32 devices in a mesh: rep: 16 (over z, y, core), zero: 2 (over x).
Axes of the slice: x: 2, y: 2, z: 4, core: 2. Of those that a mesh axis runs over, the one named last changes fastest.
Arguments:
- tokens: bfloat16 [8192, 1536], P(('rep', 'zero')), may hold values from -6 to 6
- cotangent: bfloat16 [8192, 1536], P(('rep', 'zero')), may hold values from -6 to 6
- segment_ids: int32 [8192], P(('rep', 'zero')), may hold values from 0 to 52, never falling along the last dimension, each value on 1 to 512 neighbouring positions
- master: float32 [14647296], P('zero')
- first_moment: float32 [14647296], P('zero')
- second_moment: float32 [14647296], P('zero')
- step_count: int32 [], replicated, may hold values from 1 to 20
- rates: float32 [2, 9], replicated, may hold values from 0 to 1
Outputs:
- mixed: bfloat16 [8192, 1536], P(('rep', 'zero'))
- input_grad: bfloat16 [8192, 1536], P(('rep', 'zero'))
- new_first: float32 [14647296], P('zero')
- new_second: float32 [14647296], P('zero')
- new_master: float32 [14647296], P('zero')
The draws below stay inside these ranges and needn't reach their ends.
Inputs may be any that keep to these rules, and one draw needn't show every extreme that they name: `segment_ids`: ids never fall along the tokens; a document is a run of equal ids of at most 512 tokens.
All inputs are finite; a program needn't handle non-finite values.
Results may differ from the reference program's by a relative error of at most 0.012.
Values may be sent and summed in bfloat16 or wider, within the bound.
No kernel may reach another device: no remote copies, remote signals or barrier semaphores. Data moves between devices by JAX's collectives and lax.ppermute only.
A program may use at most 512 MiB of HBM per device.

```python
import functools
import math
import jax
import jax.numpy as jnp
import numpy as np
from jax import lax

D = 1536
DI = 3072
NS = 128
HD = 64
NH = 48
E = 6448
CONV = 3328
LENGTH = 256
TOKENS = 8192
PARAMS = 14647296


def piece_bounds_drawn():
    amounts = [D * E, DI * D, 4 * CONV, CONV, D, DI, NH, NH, NH]
    bounds = [0]
    for amount in amounts:
        bounds.append(bounds[-1] + amount)
    return bounds


def by_piece(piece_values, fallback):
    position = jnp.arange(PARAMS, dtype=jnp.int32)
    bounds = piece_bounds_drawn()
    result = fallback
    for piece_index in range(9):
        inside = (position >= bounds[piece_index]) & (position < bounds[piece_index + 1])
        result = jnp.where(inside, piece_values[piece_index], result)
    return result


def gaussian_draw(key):
    return jax.random.normal(key, (PARAMS,), jnp.float32)


def gradient_scales():
    root = math.sqrt(TOKENS)
    return [0.5 * root, root, 0.5 * root, 0.5 * root, root, 0.7 * root, 4.0 * root, 4.0 * root, 4.0 * root]


def draw_master(key, part):
    subkeys = jax.random.split(jax.random.fold_in(key, 11), 2)
    gaussian = gaussian_draw(subkeys[0])
    uniform_draw = jax.random.uniform(subkeys[1], (PARAMS,), jnp.float32)
    centered = 2.0 * uniform_draw - 1.0
    small_step = jnp.exp(math.log(0.001) + uniform_draw * (math.log(0.1) - math.log(0.001)))
    step_bias = small_step + jnp.log(-jnp.expm1(-small_step))
    log_decay = jnp.log(1.0 + 15.0 * uniform_draw)
    pieces = [gaussian * D ** (-0.5), gaussian * DI ** (-0.5), 0.5 * centered, 0.5 * centered, 1.0 + 0.5 * centered, 1.0 + 0.5 * centered, step_bias, log_decay, 1.0 + 0.5 * centered]
    return by_piece(pieces, 0.02 * gaussian)


def draw_first_moment(key, part):
    gaussian = gaussian_draw(jax.random.fold_in(key, 23))
    pieces = [gaussian * factor for factor in gradient_scales()]
    return by_piece(pieces, gaussian)


def draw_second_moment(key, part):
    uniform_draw = jax.random.uniform(jax.random.fold_in(key, 37), (PARAMS,), jnp.float32)
    spread = jnp.exp(math.log(0.5) + uniform_draw * (math.log(2.0) - math.log(0.5)))
    pieces = [(spread * factor) ** 2 for factor in gradient_scales()]
    return by_piece(pieces, spread * spread)


def draw_rates(key, part):
    subkeys = jax.random.split(jax.random.fold_in(key, 53), 2)
    spreads = jnp.array([D ** (-0.5), DI ** (-0.5), 0.3, 0.3, 0.3, 0.3, 0.5, 0.5, 0.3], jnp.float32)
    learn_rate = spreads * jax.random.uniform(subkeys[0], (9,), jnp.float32, 0.3, 1.0)
    decay_rate = jax.random.uniform(subkeys[1], (9,), jnp.float32, 0.05, 0.2)
    return jnp.stack([learn_rate, decay_rate])


def shard_levels(own_key, extent, cuts, smallest, largest):
    def one(dim, blocks):
        heights = jax.random.uniform(jax.random.fold_in(jax.random.fold_in(own_key, 6), dim), (blocks,), jnp.float32, smallest / len(cuts), largest / len(cuts))
        return jnp.repeat(jnp.exp(heights), extent[dim] // blocks).reshape((-1,) + (1,) * (len(extent) - dim - 1))

    gain = one(*cuts[0])
    for cut in cuts[1:]:
        gain = gain * one(*cut)
    return gain


def profile(number_of, total, reach, slope):
    loads = [(1 << 20) // math.isqrt(rank ** slope) + 1 for rank in range(2, number_of + 1)]
    spare, holding = total - reach - (number_of - 1), [1] * (number_of - 1)
    while spare > 0:
        movable = [i for i in range(number_of - 1) if holding[i] < reach]
        mass, left = sum([loads[i] for i in movable]), spare
        for i in movable:
            addition = min(reach - holding[i], max(1, left * loads[i] // mass), spare)
            holding[i] = holding[i] + addition
            spare = spare - addition
    return np.array([reach] + holding)


def uneven(stream_key, count, total, reach, skew):
    if count == 2:
        one = jax.random.randint(stream_key, (), max(1, total - reach), min(reach, total - 1) + 1)
        return jnp.stack([one, total - one])
    tallies = jnp.asarray(profile(count, total, reach, skew), jnp.int32)
    couples = (count - 1) // 2
    donor, receiver = tallies[1:1 + 2 * couples:2], tallies[2:2 + 2 * couples:2]
    slack = jnp.minimum(donor - 1, reach - receiver)
    moved = jax.random.randint(jax.random.fold_in(stream_key, 1), (couples,), 0, 1 << 20) % (slack + 1)
    tallies = tallies.at[1:1 + 2 * couples:2].set(donor - moved).at[2:2 + 2 * couples:2].set(receiver + moved)
    return tallies[jax.random.permutation(jax.random.fold_in(stream_key, 2), count)]


def noise(key, shape, width, most, cuts=(), kind=jnp.bfloat16):
    entries = width * jax.random.normal(key, shape, jnp.float32)
    if cuts:
        entries = entries * shard_levels(key, shape, cuts, -0.22, 0.18)
    return jnp.clip(entries, -most, most).astype(kind)


def setup_inputs(seed: int = 0) -> dict:
    splits = jax.random.split(jax.random.key(seed), 9)
    tokens = noise(splits[0], (TOKENS, D), 1.0, 6.0, ((0, 32),))
    cotangent = noise(splits[1], (TOKENS, D), 1.0, 6.0, ((0, 32),))
    segment_ids = jnp.searchsorted(jnp.cumsum(uneven(splits[2], TOKENS * 5 // (LENGTH * 3), TOKENS, 2 * LENGTH, 0)), jnp.arange(TOKENS), side="right").astype(jnp.int32)
    master = draw_master(jax.random.fold_in(splits[8], 71), 0)
    first_moment = draw_first_moment(jax.random.fold_in(splits[8], 71), 0)
    second_moment = draw_second_moment(jax.random.fold_in(splits[8], 71), 0)
    step_count = jax.random.randint(splits[6], (), 1, 21).astype(jnp.int32)
    rates = draw_rates(jax.random.fold_in(splits[8], 71), 0)
    return dict(tokens=tokens, cotangent=cotangent, segment_ids=segment_ids, master=master, first_moment=first_moment, second_moment=second_moment, step_count=step_count, rates=rates)


EPSILON = 1e-05
ADAM_EPSILON = 1e-08
BETA_ONE = 0.5
BETA_TWO = 0.5
HEAD_GROUP = 4
HIGHEST = lax.Precision.HIGHEST

@jax.custom_vjp
def low(v):
    return lax.optimization_barrier(v.astype(jnp.bfloat16)).astype(jnp.float32)

@jax.custom_vjp
def low_back(v):
    return v

def low_keep(v):
    return (low(v), None)

def low_pass(kept, grad):
    return (grad,)

def back_keep(v):
    return (v, None)

def back_low(kept, grad):
    return (low(grad),)
low.defvjp(low_keep, low_pass)
low_back.defvjp(back_keep, back_low)

def piece_bounds():
    amounts = [D * E, DI * D, 4 * CONV, CONV, D, DI, NH, NH, NH]
    bounds = [0]
    for amount in amounts:
        bounds.append(bounds[-1] + amount)
    return bounds

def unpack(flat_values):
    bounds = piece_bounds()
    shapes = [(D, E), (DI, D), (4, CONV), (CONV,), (D,), (DI,), (NH,), (NH,), (NH,)]
    return tuple((flat_values[bounds[piece_index]:bounds[piece_index + 1]].reshape(shapes[piece_index]) for piece_index in range(9)))

def prenorm(residual, norm_gain):
    inverse_rms = lax.rsqrt(lax.optimization_barrier(jnp.mean(residual * residual, axis=-1, keepdims=True)) + EPSILON)
    return residual * inverse_rms * norm_gain

def head_group(contact, allowed, inputs):
    group_decay, group_step, group_values = inputs
    log_gap = group_decay[:, :, None] - group_decay[:, None, :]
    kernel = jnp.exp(jnp.where(allowed[None], log_gap, -1e+30)) * contact[None] * group_step[:, None, :]
    return jnp.einsum('gts,gsp->gtp', kernel, group_values, precision=HIGHEST)

def mixer(segment_ids, projected, filter_taps, filter_bias, step_bias, log_decay, skip_weight, gate_gain):
    length = projected.shape[0]
    gate_raw = projected[:, :DI]
    filter_in = projected[:, DI:DI + CONV]
    step_raw = projected[:, DI + CONV:]
    padded = jnp.pad(filter_in, ((3, 0), (0, 0)))
    padded_ids = jnp.pad(segment_ids, (3, 0), constant_values=-1)
    filtered = jnp.zeros_like(filter_in) + filter_bias[None, :]
    for offset in range(4):
        same_segment = (padded_ids[offset:offset + length] == segment_ids)[:, None]
        filtered = filtered + jnp.where(same_segment, padded[offset:offset + length] * filter_taps[offset][None, :], 0.0)
    activated = jax.nn.silu(filtered)
    values = activated[:, :DI].reshape(length, NH, HD)
    b_input = activated[:, DI:DI + NS]
    c_output = activated[:, DI + NS:]
    step_size = jax.nn.softplus(step_raw + step_bias[None, :])
    cumulative = jnp.cumsum(step_size * (-jnp.exp(log_decay))[None, :], axis=0)
    row_index = lax.broadcasted_iota(jnp.int32, (length, length), 0)
    col_index = lax.broadcasted_iota(jnp.int32, (length, length), 1)
    allowed = (col_index <= row_index) & (segment_ids[:, None] == segment_ids[None, :])
    contact = lax.dot_general(c_output, b_input, (((1,), (1,)), ((), ())), precision=HIGHEST)
    groups = NH // HEAD_GROUP
    grouped_decay = cumulative.T.reshape(groups, HEAD_GROUP, length)
    grouped_step = step_size.T.reshape(groups, HEAD_GROUP, length)
    grouped_values = values.transpose(1, 0, 2).reshape(groups, HEAD_GROUP, length, HD)
    scanned = lax.map(jax.checkpoint(functools.partial(head_group, contact, allowed)), (grouped_decay, grouped_step, grouped_values))
    ssd_out = scanned.reshape(NH, length, HD).transpose(1, 0, 2) + skip_weight[None, :, None] * values
    gated = ssd_out.reshape(length, DI) * jax.nn.silu(gate_raw)
    inverse_rms = lax.rsqrt(lax.optimization_barrier(jnp.mean(gated * gated, axis=-1, keepdims=True)) + EPSILON)
    return gated * inverse_rms * gate_gain

def forward(segment_ids, residual, weights):
    in_projection, out_projection, filter_taps, filter_bias, norm_gain, gate_gain, step_bias, log_decay, skip_weight = weights
    normed = low(prenorm(residual, norm_gain))
    projected = low_back(jnp.dot(normed, in_projection, precision=HIGHEST))
    mixer_out = low(mixer(segment_ids, projected, filter_taps, filter_bias, step_bias, log_decay, skip_weight, gate_gain))
    return residual + jnp.dot(mixer_out, out_projection, precision=HIGHEST)

def adamw(gradient, first_moment, second_moment, weights, start, step_count, rates):
    position = start + lax.iota(jnp.int32, gradient.shape[0])
    bounds = piece_bounds()
    learn_rate = jnp.zeros_like(gradient)
    decay_rate = jnp.zeros_like(gradient)
    for piece_index in range(9):
        inside = (position >= bounds[piece_index]) & (position < bounds[piece_index + 1])
        learn_rate = learn_rate + jnp.where(inside, rates[0, piece_index], 0.0)
        decay_rate = decay_rate + jnp.where(inside, rates[1, piece_index], 0.0)
    new_first = BETA_ONE * first_moment + (1.0 - BETA_ONE) * gradient
    new_second = BETA_TWO * second_moment + (1.0 - BETA_TWO) * gradient * gradient
    power = step_count.astype(gradient.dtype)
    correct_one = 1.0 - jnp.power(BETA_ONE, power)
    correct_two = 1.0 - jnp.power(BETA_TWO, power)
    update = new_first / correct_one / (jnp.sqrt(new_second / correct_two) + ADAM_EPSILON) + decay_rate * weights
    return (new_first, new_second, weights - learn_rate * update)

def reference(tokens, cotangent, segment_ids, master, first_moment, second_moment, step_count, rates):
    weights = unpack(low(master))
    sequences = TOKENS // LENGTH
    residual_all = tokens.astype(jnp.float32).reshape(sequences, LENGTH, D)
    cotangent_all = cotangent.astype(jnp.float32).reshape(sequences, LENGTH, D)
    ids_all = segment_ids.reshape(sequences, LENGTH)

    def one_sequence(totals, inputs):
        residual, seq_cotangent, seq_ids = inputs
        result, pullback = jax.vjp(functools.partial(forward, seq_ids), residual, weights)
        grad_residual, grad_weights = pullback(seq_cotangent)
        totals = jax.tree.map(jnp.add, totals, grad_weights)
        return (totals, (result, grad_residual))
    zero_totals = tuple((jnp.zeros_like(weight) for weight in weights))
    totals, (results, grads) = lax.scan(one_sequence, zero_totals, (residual_all, cotangent_all, ids_all))
    mixed = results.reshape(TOKENS, D).astype(jnp.bfloat16)
    input_grad = grads.reshape(TOKENS, D).astype(jnp.bfloat16)
    used = piece_bounds()[-1]
    gradient = jnp.concatenate([total.reshape(-1) for total in totals] + [jnp.zeros((PARAMS - used,), jnp.float32)])
    new_first, new_second, new_master = adamw(gradient, first_moment, second_moment, master, 0, step_count, rates)
    return (mixed, input_grad, new_first, new_second, new_master)
```

```python
import functools

import jax
import jax.numpy as jnp
from jax import lax
from jax.sharding import PartitionSpec as P

D = 1536
DI = 3072
NS = 128
HD = 64
NH = 48
E = 6448
CONV = 3328


EPSILON = 1e-05
ADAM_EPSILON = 1e-08
BETA_ONE = 0.5
BETA_TWO = 0.5
HEAD_GROUP = 4
HIGHEST = lax.Precision.HIGHEST


def piece_bounds():
    amounts = [D * E, DI * D, 4 * CONV, CONV, D, DI, NH, NH, NH]
    bounds = [0]
    for amount in amounts:
        bounds.append(bounds[-1] + amount)
    return bounds


def unpack(flat_values):
    bounds = piece_bounds()
    shapes = [(D, E), (DI, D), (4, CONV), (CONV,), (D,), (DI,), (NH,), (NH,), (NH,)]
    return tuple(
        (
            flat_values[bounds[piece_index] : bounds[piece_index + 1]].reshape(shapes[piece_index])
            for piece_index in range(9)
        )
    )


def contract(left, right, left_dim, right_dim):
    return lax.dot_general(
        left, right, (((left_dim,), (right_dim,)), ((), ())), preferred_element_type=jnp.float32
    )


def prenorm(residual, norm_gain):
    inverse_rms = lax.rsqrt(jnp.mean(residual * residual, axis=-1, keepdims=True) + EPSILON)
    return residual * inverse_rms * norm_gain


def head_group(contact, allowed, inputs):
    group_decay, group_step, group_values = inputs
    log_gap = group_decay[:, :, None] - group_decay[:, None, :]
    kernel = (
        jnp.exp(jnp.where(allowed[None], log_gap, -1e30)) * contact[None] * group_step[:, None, :]
    )
    return jnp.einsum("gts,gsp->gtp", kernel, group_values, precision=HIGHEST)


def mixer(
    segment_ids, projected, filter_taps, filter_bias, step_bias, log_decay, skip_weight, gate_gain
):
    length = projected.shape[0]
    gate_raw = projected[:, :DI]
    filter_in = projected[:, DI : DI + CONV]
    step_raw = projected[:, DI + CONV :]
    padded = jnp.pad(filter_in, ((3, 0), (0, 0)))
    padded_ids = jnp.pad(segment_ids, (3, 0), constant_values=-1)
    filtered = jnp.zeros_like(filter_in) + filter_bias[None, :]
    for offset in range(4):
        same_segment = (padded_ids[offset : offset + length] == segment_ids)[:, None]
        filtered = filtered + jnp.where(
            same_segment, padded[offset : offset + length] * filter_taps[offset][None, :], 0.0
        )
    activated = jax.nn.silu(filtered)
    values = activated[:, :DI].reshape(length, NH, HD)
    b_input = activated[:, DI : DI + NS]
    c_output = activated[:, DI + NS :]
    step_size = jax.nn.softplus(step_raw + step_bias[None, :])
    cumulative = jnp.cumsum(step_size * (-jnp.exp(log_decay))[None, :], axis=0)
    row_index = lax.broadcasted_iota(jnp.int32, (length, length), 0)
    col_index = lax.broadcasted_iota(jnp.int32, (length, length), 1)
    allowed = (col_index <= row_index) & (segment_ids[:, None] == segment_ids[None, :])
    contact = lax.dot_general(c_output, b_input, (((1,), (1,)), ((), ())), precision=HIGHEST)
    groups = NH // HEAD_GROUP
    grouped_decay = cumulative.T.reshape(groups, HEAD_GROUP, length)
    grouped_step = step_size.T.reshape(groups, HEAD_GROUP, length)
    grouped_values = values.transpose(1, 0, 2).reshape(groups, HEAD_GROUP, length, HD)
    scanned = lax.map(
        jax.checkpoint(functools.partial(head_group, contact, allowed)),
        (grouped_decay, grouped_step, grouped_values),
    )
    ssd_out = (
        scanned.reshape(NH, length, HD).transpose(1, 0, 2) + skip_weight[None, :, None] * values
    )
    gated = ssd_out.reshape(length, DI) * jax.nn.silu(gate_raw)
    inverse_rms = lax.rsqrt(jnp.mean(gated * gated, axis=-1, keepdims=True) + EPSILON)
    return gated * inverse_rms * gate_gain


def adamw(gradient, first_moment, second_moment, weights, start, step_count, rates):
    position = start + lax.iota(jnp.int32, gradient.shape[0])
    bounds = piece_bounds()
    learn_rate = jnp.zeros_like(gradient)
    decay_rate = jnp.zeros_like(gradient)
    for piece_index in range(9):
        inside = (position >= bounds[piece_index]) & (position < bounds[piece_index + 1])
        learn_rate = learn_rate + jnp.where(inside, rates[0, piece_index], 0.0)
        decay_rate = decay_rate + jnp.where(inside, rates[1, piece_index], 0.0)
    new_first = BETA_ONE * first_moment + (1.0 - BETA_ONE) * gradient
    new_second = BETA_TWO * second_moment + (1.0 - BETA_TWO) * gradient * gradient
    power = step_count.astype(gradient.dtype)
    correct_one = 1.0 - jnp.power(BETA_ONE, power)
    correct_two = 1.0 - jnp.power(BETA_TWO, power)
    update = (
        new_first / correct_one / (jnp.sqrt(new_second / correct_two) + ADAM_EPSILON)
        + decay_rate * weights
    )
    return (new_first, new_second, weights - learn_rate * update)


def gather_weights(master):
    rep_size = lax.axis_size("rep")
    zero_size = lax.axis_size("zero")
    shard_size = master.shape[0]
    piece_size = shard_size // rep_size
    rep_index = lax.axis_index("rep")
    zero_index = lax.axis_index("zero")
    mine = lax.dynamic_slice_in_dim(master, rep_index * piece_size, piece_size).astype(jnp.bfloat16)
    across = lax.all_gather(mine, "zero", axis=0, tiled=False)
    if zero_size > 1:
        picks = (zero_index + 1 + jnp.arange(zero_size - 1)) % zero_size
        others = jnp.take(across, picks, axis=0)
        spread = lax.all_gather(others, "rep", axis=0, tiled=False)
        others_flat = spread.transpose(1, 0, 2).reshape(zero_size - 1, shard_size)
        stacked = jnp.concatenate([master.astype(jnp.bfloat16)[None], others_flat], axis=0)
        stacked = jnp.roll(stacked, zero_index, axis=0)
    else:
        stacked = master.astype(jnp.bfloat16)[None]
    return stacked.reshape(-1)


def reduce_gradient(pieces, shard_size):
    zero_size = lax.axis_size("zero")
    total_params = shard_size * zero_size
    used = piece_bounds()[-1]
    flat_grad = jnp.concatenate(
        [piece_grad.reshape(-1).astype(jnp.bfloat16) for piece_grad in pieces]
        + [jnp.zeros((total_params - used,), jnp.bfloat16)]
    )
    summed = lax.psum(flat_grad, ("rep", "zero"))
    return lax.dynamic_slice_in_dim(summed, lax.axis_index("zero") * shard_size, shard_size)


def body(tokens, cotangent, segment_ids, master, first_moment, second_moment, step_count, rates):
    gathered = gather_weights(master)
    (
        in_projection,
        out_projection,
        filter_taps,
        filter_bias,
        norm_gain,
        gate_gain,
        step_bias,
        log_decay,
        skip_weight,
    ) = unpack(gathered)
    residual = tokens.astype(jnp.float32)
    normed, norm_pullback = jax.vjp(prenorm, residual, norm_gain.astype(jnp.float32))
    normed_low = normed.astype(jnp.bfloat16)
    projected = jnp.dot(normed_low, in_projection, preferred_element_type=jnp.float32)
    mixer_out, mixer_pullback = jax.vjp(
        functools.partial(mixer, segment_ids),
        projected,
        filter_taps.astype(jnp.float32),
        filter_bias.astype(jnp.float32),
        step_bias.astype(jnp.float32),
        log_decay.astype(jnp.float32),
        skip_weight.astype(jnp.float32),
        gate_gain.astype(jnp.float32),
    )
    mixer_low = mixer_out.astype(jnp.bfloat16)
    branch = jnp.dot(mixer_low, out_projection, preferred_element_type=jnp.float32)
    mixed = (residual + branch).astype(jnp.bfloat16)
    grad_out = contract(mixer_low, cotangent, 0, 0)
    grad_mixer = contract(cotangent, out_projection, 1, 1)
    grad_projected, grad_taps, grad_bias, grad_step_bias, grad_decay, grad_skip, grad_gate_gain = (
        mixer_pullback(grad_mixer)
    )
    projected_low = grad_projected.astype(jnp.bfloat16)
    grad_in = contract(normed_low, projected_low, 0, 0)
    grad_normed = contract(projected_low, in_projection, 1, 1)
    grad_residual, grad_norm_gain = norm_pullback(grad_normed)
    input_grad = (cotangent.astype(jnp.float32) + grad_residual).astype(jnp.bfloat16)
    pieces = [
        grad_in,
        grad_out,
        grad_taps,
        grad_bias,
        grad_norm_gain,
        grad_gate_gain,
        grad_step_bias,
        grad_decay,
        grad_skip,
    ]
    shard_size = master.shape[0]
    gradient = reduce_gradient(pieces, shard_size).astype(jnp.float32)
    shard_start = lax.axis_index("zero") * shard_size
    new_first, new_second, new_master = adamw(
        gradient, first_moment, second_moment, master, shard_start, step_count, rates
    )
    return (mixed, input_grad, new_first, new_second, new_master)


def solution(mesh):
    in_specs = (
        P(("rep", "zero"), None),
        P(("rep", "zero"), None),
        P(("rep", "zero")),
        P("zero"),
        P("zero"),
        P("zero"),
        P(),
        P(),
    )
    out_specs = (
        P(("rep", "zero"), None),
        P(("rep", "zero"), None),
        P("zero"),
        P("zero"),
        P("zero"),
    )
    return jax.shard_map(body, mesh=mesh, in_specs=in_specs, out_specs=out_specs, check_vma=False)
```

```python
import functools

import jax
import jax.numpy as jnp
from jax import lax
from jax.sharding import PartitionSpec as P

D = 1536
DI = 3072
NS = 128
HD = 64
NH = 48
E = 6448
CONV = 3328


EPSILON = 1e-05
ADAM_EPSILON = 1e-08
BETA_ONE = 0.5
BETA_TWO = 0.5
HEAD_GROUP = 4
HIGHEST = lax.Precision.HIGHEST


def piece_bounds():
    amounts = [D * E, DI * D, 4 * CONV, CONV, D, DI, NH, NH, NH]
    bounds = [0]
    for amount in amounts:
        bounds.append(bounds[-1] + amount)
    return bounds


def unpack(flat_values):
    bounds = piece_bounds()
    shapes = [(D, E), (DI, D), (4, CONV), (CONV,), (D,), (DI,), (NH,), (NH,), (NH,)]
    return tuple(
        (
            flat_values[bounds[piece_index] : bounds[piece_index + 1]].reshape(shapes[piece_index])
            for piece_index in range(9)
        )
    )


def contract(left, right, left_dim, right_dim):
    return lax.dot_general(
        left, right, (((left_dim,), (right_dim,)), ((), ())), preferred_element_type=jnp.float32
    )


def prenorm(residual, norm_gain):
    inverse_rms = lax.rsqrt(jnp.mean(residual * residual, axis=-1, keepdims=True) + EPSILON)
    return residual * inverse_rms * norm_gain


def head_group(contact, allowed, inputs):
    group_decay, group_step, group_values = inputs
    log_gap = group_decay[:, :, None] - group_decay[:, None, :]
    kernel = (
        jnp.exp(jnp.where(allowed[None], log_gap, -1e30)) * contact[None] * group_step[:, None, :]
    )
    return jnp.einsum("gts,gsp->gtp", kernel, group_values, precision=HIGHEST)


def mixer(
    segment_ids, projected, filter_taps, filter_bias, step_bias, log_decay, skip_weight, gate_gain
):
    length = projected.shape[0]
    gate_raw = projected[:, :DI]
    filter_in = projected[:, DI : DI + CONV]
    step_raw = projected[:, DI + CONV :]
    padded = jnp.pad(filter_in, ((3, 0), (0, 0)))
    padded_ids = jnp.pad(segment_ids, (3, 0), constant_values=-1)
    filtered = jnp.zeros_like(filter_in) + filter_bias[None, :]
    for offset in range(4):
        same_segment = (padded_ids[offset : offset + length] == segment_ids)[:, None]
        filtered = filtered + jnp.where(
            same_segment, padded[offset : offset + length] * filter_taps[offset][None, :], 0.0
        )
    activated = jax.nn.silu(filtered)
    values = activated[:, :DI].reshape(length, NH, HD)
    b_input = activated[:, DI : DI + NS]
    c_output = activated[:, DI + NS :]
    step_size = jax.nn.softplus(step_raw + step_bias[None, :])
    cumulative = jnp.cumsum(step_size * (-jnp.exp(log_decay))[None, :], axis=0)
    row_index = lax.broadcasted_iota(jnp.int32, (length, length), 0)
    col_index = lax.broadcasted_iota(jnp.int32, (length, length), 1)
    allowed = (col_index <= row_index) & (segment_ids[:, None] == segment_ids[None, :])
    contact = lax.dot_general(c_output, b_input, (((1,), (1,)), ((), ())), precision=HIGHEST)
    groups = NH // HEAD_GROUP
    grouped_decay = cumulative.T.reshape(groups, HEAD_GROUP, length)
    grouped_step = step_size.T.reshape(groups, HEAD_GROUP, length)
    grouped_values = values.transpose(1, 0, 2).reshape(groups, HEAD_GROUP, length, HD)
    scanned = lax.map(
        jax.checkpoint(functools.partial(head_group, contact, allowed)),
        (grouped_decay, grouped_step, grouped_values),
    )
    ssd_out = (
        scanned.reshape(NH, length, HD).transpose(1, 0, 2) + skip_weight[None, :, None] * values
    )
    gated = ssd_out.reshape(length, DI) * jax.nn.silu(gate_raw)
    inverse_rms = lax.rsqrt(jnp.mean(gated * gated, axis=-1, keepdims=True) + EPSILON)
    return gated * inverse_rms * gate_gain


def adamw(gradient, first_moment, second_moment, weights, start, step_count, rates):
    position = start + lax.iota(jnp.int32, gradient.shape[0])
    bounds = piece_bounds()
    learn_rate = jnp.zeros_like(gradient)
    decay_rate = jnp.zeros_like(gradient)
    for piece_index in range(9):
        inside = (position >= bounds[piece_index]) & (position < bounds[piece_index + 1])
        learn_rate = learn_rate + jnp.where(inside, rates[0, piece_index], 0.0)
        decay_rate = decay_rate + jnp.where(inside, rates[1, piece_index], 0.0)
    new_first = BETA_ONE * first_moment + (1.0 - BETA_ONE) * gradient
    new_second = BETA_TWO * second_moment + (1.0 - BETA_TWO) * gradient * gradient
    power = step_count.astype(gradient.dtype)
    correct_one = 1.0 - jnp.power(BETA_ONE, power)
    correct_two = 1.0 - jnp.power(BETA_TWO, power)
    update = (
        new_first / correct_one / (jnp.sqrt(new_second / correct_two) + ADAM_EPSILON)
        + decay_rate * weights
    )
    return (new_first, new_second, weights - learn_rate * update)


def gather_weights(master):
    rep_size = lax.axis_size("rep")
    zero_size = lax.axis_size("zero")
    shard_size = master.shape[0]
    piece_size = shard_size // rep_size
    rep_index = lax.axis_index("rep")
    zero_index = lax.axis_index("zero")
    own = master.astype(jnp.bfloat16)
    mine = lax.dynamic_slice_in_dim(own, rep_index * piece_size, piece_size)
    across = lax.all_gather(mine, "zero", axis=0, tiled=False)
    if zero_size == 2:
        other_piece = lax.dynamic_index_in_dim(across, 1 - zero_index, 0, keepdims=False)
        other = lax.all_gather(other_piece, "rep", axis=0, tiled=True)
        shards = [
            jnp.where(zero_index == 0, own, other),
            jnp.where(zero_index == 0, other, own),
        ]
    else:
        shards = [
            lax.all_gather(across[shard], "rep", axis=0, tiled=True)
            for shard in range(zero_size)
        ]
    return jnp.concatenate(shards)


def reduce_gradient(pieces, shard_size):
    zero_size = lax.axis_size("zero")
    total_params = shard_size * zero_size
    used = piece_bounds()[-1]
    flat = [piece_grad.reshape(-1).astype(jnp.bfloat16) for piece_grad in pieces]
    tail = jnp.concatenate(flat[3:] + [jnp.zeros((total_params - used,), jnp.bfloat16)])
    flat_grad = jnp.concatenate(flat[:3] + [tail])
    summed = lax.psum(flat_grad, ("rep", "zero"))
    return lax.dynamic_slice_in_dim(summed, lax.axis_index("zero") * shard_size, shard_size)


def body(tokens, cotangent, segment_ids, master, first_moment, second_moment, step_count, rates):
    gathered = gather_weights(master)
    (
        in_projection,
        out_projection,
        filter_taps,
        filter_bias,
        norm_gain,
        gate_gain,
        step_bias,
        log_decay,
        skip_weight,
    ) = unpack(gathered)
    residual = tokens.astype(jnp.float32)
    normed, norm_pullback = jax.vjp(prenorm, residual, norm_gain.astype(jnp.float32))
    normed_low = normed.astype(jnp.bfloat16)
    projected = jnp.dot(normed_low, in_projection, preferred_element_type=jnp.float32)
    mixer_out, mixer_pullback = jax.vjp(
        functools.partial(mixer, segment_ids),
        projected,
        filter_taps.astype(jnp.float32),
        filter_bias.astype(jnp.float32),
        step_bias.astype(jnp.float32),
        log_decay.astype(jnp.float32),
        skip_weight.astype(jnp.float32),
        gate_gain.astype(jnp.float32),
    )
    mixer_low = mixer_out.astype(jnp.bfloat16)
    branch = jnp.dot(mixer_low, out_projection, preferred_element_type=jnp.float32)
    mixed = (residual + branch).astype(jnp.bfloat16)
    grad_out = contract(mixer_low, cotangent, 0, 0)
    grad_mixer = contract(cotangent, out_projection, 1, 1)
    grad_projected, grad_taps, grad_bias, grad_step_bias, grad_decay, grad_skip, grad_gate_gain = (
        mixer_pullback(grad_mixer)
    )
    projected_low = grad_projected.astype(jnp.bfloat16)
    grad_in = contract(normed_low, projected_low, 0, 0)
    grad_normed = contract(projected_low, in_projection, 1, 1)
    grad_residual, grad_norm_gain = norm_pullback(grad_normed)
    input_grad = (cotangent.astype(jnp.float32) + grad_residual).astype(jnp.bfloat16)
    pieces = [
        grad_in,
        grad_out,
        grad_taps,
        grad_bias,
        grad_norm_gain,
        grad_gate_gain,
        grad_step_bias,
        grad_decay,
        grad_skip,
    ]
    shard_size = master.shape[0]
    gradient = reduce_gradient(pieces, shard_size).astype(jnp.float32)
    shard_start = lax.axis_index("zero") * shard_size
    new_first, new_second, new_master = adamw(
        gradient, first_moment, second_moment, master, shard_start, step_count, rates
    )
    return (mixed, input_grad, new_first, new_second, new_master)


def solution(mesh):
    in_specs = (
        P(("rep", "zero"), None),
        P(("rep", "zero"), None),
        P(("rep", "zero")),
        P("zero"),
        P("zero"),
        P("zero"),
        P(),
        P(),
    )
    out_specs = (
        P(("rep", "zero"), None),
        P(("rep", "zero"), None),
        P("zero"),
        P("zero"),
        P("zero"),
    )
    return jax.shard_map(body, mesh=mesh, in_specs=in_specs, out_specs=out_specs, check_vma=False)
```

```python
import functools

import jax
import jax.numpy as jnp
from jax import lax
from jax.sharding import PartitionSpec as P

D = 1536
DI = 3072
NS = 128
HD = 64
NH = 48
E = 6448
CONV = 3328


EPSILON = 1e-05
ADAM_EPSILON = 1e-08
BETA_ONE = 0.5
BETA_TWO = 0.5
HEAD_GROUP = 4
HIGHEST = lax.Precision.HIGHEST


def piece_bounds():
    amounts = [D * E, DI * D, 4 * CONV, CONV, D, DI, NH, NH, NH]
    bounds = [0]
    for amount in amounts:
        bounds.append(bounds[-1] + amount)
    return bounds


def unpack(flat_values):
    bounds = piece_bounds()
    shapes = [(D, E), (DI, D), (4, CONV), (CONV,), (D,), (DI,), (NH,), (NH,), (NH,)]
    return tuple(
        (
            flat_values[bounds[piece_index] : bounds[piece_index + 1]].reshape(shapes[piece_index])
            for piece_index in range(9)
        )
    )


def contract(left, right, left_dim, right_dim):
    return lax.dot_general(
        left, right, (((left_dim,), (right_dim,)), ((), ())), preferred_element_type=jnp.float32
    )


def prenorm(residual, norm_gain):
    inverse_rms = lax.rsqrt(jnp.mean(residual * residual, axis=-1, keepdims=True) + EPSILON)
    return residual * inverse_rms * norm_gain


def head_group(contact, allowed, inputs):
    group_decay, group_step, group_values = inputs
    log_gap = group_decay[:, :, None] - group_decay[:, None, :]
    kernel = (
        jnp.exp(jnp.where(allowed[None], log_gap, -1e30)) * contact[None] * group_step[:, None, :]
    )
    return jnp.einsum("gts,gsp->gtp", kernel, group_values, precision=HIGHEST)


def mixer(
    segment_ids, projected, filter_taps, filter_bias, step_bias, log_decay, skip_weight, gate_gain
):
    length = projected.shape[0]
    gate_raw = projected[:, :DI]
    filter_in = projected[:, DI : DI + CONV]
    step_raw = projected[:, DI + CONV :]
    padded = jnp.pad(filter_in, ((3, 0), (0, 0)))
    padded_ids = jnp.pad(segment_ids, (3, 0), constant_values=-1)
    filtered = jnp.zeros_like(filter_in) + filter_bias[None, :]
    for offset in range(4):
        same_segment = (padded_ids[offset : offset + length] == segment_ids)[:, None]
        filtered = filtered + jnp.where(
            same_segment, padded[offset : offset + length] * filter_taps[offset][None, :], 0.0
        )
    activated = jax.nn.silu(filtered)
    values = activated[:, :DI].reshape(length, NH, HD)
    b_input = activated[:, DI : DI + NS]
    c_output = activated[:, DI + NS :]
    step_size = jax.nn.softplus(step_raw + step_bias[None, :])
    cumulative = jnp.cumsum(step_size * (-jnp.exp(log_decay))[None, :], axis=0)
    row_index = lax.broadcasted_iota(jnp.int32, (length, length), 0)
    col_index = lax.broadcasted_iota(jnp.int32, (length, length), 1)
    allowed = (col_index <= row_index) & (segment_ids[:, None] == segment_ids[None, :])
    contact = lax.dot_general(c_output, b_input, (((1,), (1,)), ((), ())), precision=HIGHEST)
    groups = NH // HEAD_GROUP
    grouped_decay = cumulative.T.reshape(groups, HEAD_GROUP, length)
    grouped_step = step_size.T.reshape(groups, HEAD_GROUP, length)
    grouped_values = values.transpose(1, 0, 2).reshape(groups, HEAD_GROUP, length, HD)
    scanned = lax.map(
        jax.checkpoint(functools.partial(head_group, contact, allowed)),
        (grouped_decay, grouped_step, grouped_values),
    )
    ssd_out = (
        scanned.reshape(NH, length, HD).transpose(1, 0, 2) + skip_weight[None, :, None] * values
    )
    gated = ssd_out.reshape(length, DI) * jax.nn.silu(gate_raw)
    inverse_rms = lax.rsqrt(jnp.mean(gated * gated, axis=-1, keepdims=True) + EPSILON)
    return gated * inverse_rms * gate_gain


def adamw(gradient, first_moment, second_moment, weights, start, step_count, rates):
    position = start + lax.iota(jnp.int32, gradient.shape[0])
    bounds = piece_bounds()
    learn_rate = jnp.zeros_like(gradient)
    decay_rate = jnp.zeros_like(gradient)
    for piece_index in range(9):
        inside = (position >= bounds[piece_index]) & (position < bounds[piece_index + 1])
        learn_rate = learn_rate + jnp.where(inside, rates[0, piece_index], 0.0)
        decay_rate = decay_rate + jnp.where(inside, rates[1, piece_index], 0.0)
    new_first = BETA_ONE * first_moment + (1.0 - BETA_ONE) * gradient
    new_second = BETA_TWO * second_moment + (1.0 - BETA_TWO) * gradient * gradient
    power = step_count.astype(gradient.dtype)
    correct_one = 1.0 - jnp.power(BETA_ONE, power)
    correct_two = 1.0 - jnp.power(BETA_TWO, power)
    update = (
        new_first / correct_one / (jnp.sqrt(new_second / correct_two) + ADAM_EPSILON)
        + decay_rate * weights
    )
    return (new_first, new_second, weights - learn_rate * update)


def gather_weights(master):
    rep_size = lax.axis_size("rep")
    zero_size = lax.axis_size("zero")
    shard_size = master.shape[0]
    piece_size = shard_size // rep_size
    rep_index = lax.axis_index("rep")
    zero_index = lax.axis_index("zero")
    own = master.astype(jnp.bfloat16)
    mine = lax.dynamic_slice_in_dim(own, rep_index * piece_size, piece_size)
    if zero_size == 2:
        other_piece = lax.ppermute(mine, "zero", [(0, 1), (1, 0)])
        other = lax.all_gather(other_piece, "rep", axis=0, tiled=True)
        shards = [
            jnp.where(zero_index == 0, own, other),
            jnp.where(zero_index == 0, other, own),
        ]
    else:
        across = lax.all_gather(mine, "zero", axis=0, tiled=True)
        shards = [
            lax.all_gather(
                lax.dynamic_slice_in_dim(across, shard * piece_size, piece_size),
                "rep",
                axis=0,
                tiled=True,
            )
            for shard in range(zero_size)
        ]
    return jnp.concatenate(shards)


def reduce_gradient(pieces, shard_size):
    zero_size = lax.axis_size("zero")
    total_params = shard_size * zero_size
    flat_grad = jnp.zeros((total_params,), jnp.bfloat16)
    offset = 0
    for piece_grad in pieces:
        flat_piece = piece_grad.reshape(-1).astype(jnp.bfloat16)
        flat_grad = lax.dynamic_update_slice_in_dim(flat_grad, flat_piece, offset, 0)
        offset += flat_piece.shape[0]
    summed = lax.psum(flat_grad, ("rep", "zero"))
    return lax.dynamic_slice_in_dim(summed, lax.axis_index("zero") * shard_size, shard_size)


def body(tokens, cotangent, segment_ids, master, first_moment, second_moment, step_count, rates):
    gathered = gather_weights(master)
    (
        in_projection,
        out_projection,
        filter_taps,
        filter_bias,
        norm_gain,
        gate_gain,
        step_bias,
        log_decay,
        skip_weight,
    ) = unpack(gathered)
    residual = tokens.astype(jnp.float32)
    normed, norm_pullback = jax.vjp(prenorm, residual, norm_gain.astype(jnp.float32))
    normed_low = normed.astype(jnp.bfloat16)
    projected = jnp.dot(normed_low, in_projection, preferred_element_type=jnp.float32)
    mixer_out, mixer_pullback = jax.vjp(
        functools.partial(mixer, segment_ids),
        projected,
        filter_taps.astype(jnp.float32),
        filter_bias.astype(jnp.float32),
        step_bias.astype(jnp.float32),
        log_decay.astype(jnp.float32),
        skip_weight.astype(jnp.float32),
        gate_gain.astype(jnp.float32),
    )
    mixer_low = mixer_out.astype(jnp.bfloat16)
    branch = jnp.dot(mixer_low, out_projection, preferred_element_type=jnp.float32)
    mixed = (residual + branch).astype(jnp.bfloat16)
    grad_out = contract(mixer_low, cotangent, 0, 0)
    grad_mixer = contract(cotangent, out_projection, 1, 1)
    grad_projected, grad_taps, grad_bias, grad_step_bias, grad_decay, grad_skip, grad_gate_gain = (
        mixer_pullback(grad_mixer)
    )
    projected_low = grad_projected.astype(jnp.bfloat16)
    grad_in = contract(normed_low, projected_low, 0, 0)
    grad_normed = contract(projected_low, in_projection, 1, 1)
    grad_residual, grad_norm_gain = norm_pullback(grad_normed)
    input_grad = (cotangent.astype(jnp.float32) + grad_residual).astype(jnp.bfloat16)
    pieces = [
        grad_in,
        grad_out,
        grad_taps,
        grad_bias,
        grad_norm_gain,
        grad_gate_gain,
        grad_step_bias,
        grad_decay,
        grad_skip,
    ]
    shard_size = master.shape[0]
    gradient = reduce_gradient(pieces, shard_size).astype(jnp.float32)
    shard_start = lax.axis_index("zero") * shard_size
    new_first, new_second, new_master = adamw(
        gradient, first_moment, second_moment, master, shard_start, step_count, rates
    )
    return (mixed, input_grad, new_first, new_second, new_master)


def solution(mesh):
    in_specs = (
        P(("rep", "zero"), None),
        P(("rep", "zero"), None),
        P(("rep", "zero")),
        P("zero"),
        P("zero"),
        P("zero"),
        P(),
        P(),
    )
    out_specs = (
        P(("rep", "zero"), None),
        P(("rep", "zero"), None),
        P("zero"),
        P("zero"),
        P("zero"),
    )
    return jax.shard_map(body, mesh=mesh, in_specs=in_specs, out_specs=out_specs, check_vma=False)
```

```python
import functools

import jax
import jax.numpy as jnp
from jax import lax
from jax.sharding import PartitionSpec as P

D = 1536
DI = 3072
NS = 128
HD = 64
NH = 48
E = 6448
CONV = 3328


EPSILON = 1e-05
ADAM_EPSILON = 1e-08
BETA_ONE = 0.5
BETA_TWO = 0.5
HEAD_GROUP = 4
HIGHEST = lax.Precision.HIGHEST


def piece_bounds():
    amounts = [D * E, DI * D, 4 * CONV, CONV, D, DI, NH, NH, NH]
    bounds = [0]
    for amount in amounts:
        bounds.append(bounds[-1] + amount)
    return bounds


def unpack(flat_values):
    bounds = piece_bounds()
    shapes = [(D, E), (DI, D), (4, CONV), (CONV,), (D,), (DI,), (NH,), (NH,), (NH,)]
    return tuple(
        (
            flat_values[bounds[piece_index] : bounds[piece_index + 1]].reshape(shapes[piece_index])
            for piece_index in range(9)
        )
    )


def contract(left, right, left_dim, right_dim):
    return lax.dot_general(
        left, right, (((left_dim,), (right_dim,)), ((), ())), preferred_element_type=jnp.float32
    )


def prenorm(residual, norm_gain):
    inverse_rms = lax.rsqrt(jnp.mean(residual * residual, axis=-1, keepdims=True) + EPSILON)
    return residual * inverse_rms * norm_gain


def head_group(contact, allowed, inputs):
    group_decay, group_step, group_values = inputs
    log_gap = group_decay[:, :, None] - group_decay[:, None, :]
    kernel = (
        jnp.exp(jnp.where(allowed[None], log_gap, -1e30)) * contact[None] * group_step[:, None, :]
    )
    return jnp.einsum("gts,gsp->gtp", kernel, group_values, precision=HIGHEST)


def mixer(
    segment_ids, projected, filter_taps, filter_bias, step_bias, log_decay, skip_weight, gate_gain
):
    length = projected.shape[0]
    gate_raw = projected[:, :DI]
    filter_in = projected[:, DI : DI + CONV]
    step_raw = projected[:, DI + CONV :]
    padded = jnp.pad(filter_in, ((3, 0), (0, 0)))
    padded_ids = jnp.pad(segment_ids, (3, 0), constant_values=-1)
    filtered = jnp.zeros_like(filter_in) + filter_bias[None, :]
    for offset in range(4):
        same_segment = (padded_ids[offset : offset + length] == segment_ids)[:, None]
        filtered = filtered + jnp.where(
            same_segment, padded[offset : offset + length] * filter_taps[offset][None, :], 0.0
        )
    activated = jax.nn.silu(filtered)
    values = activated[:, :DI].reshape(length, NH, HD)
    b_input = activated[:, DI : DI + NS]
    c_output = activated[:, DI + NS :]
    step_size = jax.nn.softplus(step_raw + step_bias[None, :])
    cumulative = jnp.cumsum(step_size * (-jnp.exp(log_decay))[None, :], axis=0)
    row_index = lax.broadcasted_iota(jnp.int32, (length, length), 0)
    col_index = lax.broadcasted_iota(jnp.int32, (length, length), 1)
    allowed = (col_index <= row_index) & (segment_ids[:, None] == segment_ids[None, :])
    contact = lax.dot_general(c_output, b_input, (((1,), (1,)), ((), ())), precision=HIGHEST)
    groups = NH // HEAD_GROUP
    grouped_decay = cumulative.T.reshape(groups, HEAD_GROUP, length)
    grouped_step = step_size.T.reshape(groups, HEAD_GROUP, length)
    grouped_values = values.transpose(1, 0, 2).reshape(groups, HEAD_GROUP, length, HD)
    scanned = lax.map(
        jax.checkpoint(functools.partial(head_group, contact, allowed)),
        (grouped_decay, grouped_step, grouped_values),
    )
    ssd_out = (
        scanned.reshape(NH, length, HD).transpose(1, 0, 2) + skip_weight[None, :, None] * values
    )
    gated = ssd_out.reshape(length, DI) * jax.nn.silu(gate_raw)
    inverse_rms = lax.rsqrt(jnp.mean(gated * gated, axis=-1, keepdims=True) + EPSILON)
    return gated * inverse_rms * gate_gain


def adamw(gradient, first_moment, second_moment, weights, start, step_count, rates):
    position = start + lax.iota(jnp.int32, gradient.shape[0])
    bounds = piece_bounds()
    learn_rate = jnp.zeros_like(gradient)
    decay_rate = jnp.zeros_like(gradient)
    for piece_index in range(9):
        inside = (position >= bounds[piece_index]) & (position < bounds[piece_index + 1])
        learn_rate = learn_rate + jnp.where(inside, rates[0, piece_index], 0.0)
        decay_rate = decay_rate + jnp.where(inside, rates[1, piece_index], 0.0)
    new_first = BETA_ONE * first_moment + (1.0 - BETA_ONE) * gradient
    new_second = BETA_TWO * second_moment + (1.0 - BETA_TWO) * gradient * gradient
    power = step_count.astype(gradient.dtype)
    correct_one = 1.0 - jnp.power(BETA_ONE, power)
    correct_two = 1.0 - jnp.power(BETA_TWO, power)
    update = (
        new_first / correct_one / (jnp.sqrt(new_second / correct_two) + ADAM_EPSILON)
        + decay_rate * weights
    )
    return (new_first, new_second, weights - learn_rate * update)


def gather_weights(master):
    rep_size = lax.axis_size("rep")
    zero_size = lax.axis_size("zero")
    shard_size = master.shape[0]
    piece_size = shard_size // rep_size
    rep_index = lax.axis_index("rep")
    zero_index = lax.axis_index("zero")
    own = master.astype(jnp.bfloat16)
    mine = lax.dynamic_slice_in_dim(own, rep_index * piece_size, piece_size)
    if zero_size == 2:
        other_piece = lax.ppermute(mine, "zero", [(0, 1), (1, 0)])
        other = lax.all_gather(other_piece, "rep", axis=0, tiled=True)
        shards = [
            jnp.where(zero_index == 0, own, other),
            jnp.where(zero_index == 0, other, own),
        ]
    else:
        across = lax.all_gather(mine, "zero", axis=0, tiled=True)
        shards = [
            lax.all_gather(
                lax.dynamic_slice_in_dim(across, shard * piece_size, piece_size),
                "rep",
                axis=0,
                tiled=True,
            )
            for shard in range(zero_size)
        ]
    return jnp.concatenate(shards)


def assemble_gradient(summed_pieces, shard_size):
    zero_size = lax.axis_size("zero")
    total_params = shard_size * zero_size
    flat_grad = jnp.zeros((total_params,), jnp.bfloat16)
    offset = 0
    for flat_piece in summed_pieces:
        flat_grad = lax.dynamic_update_slice_in_dim(flat_grad, flat_piece, offset, 0)
        offset += flat_piece.shape[0]
    return lax.dynamic_slice_in_dim(flat_grad, lax.axis_index("zero") * shard_size, shard_size)


def flat_low(piece_grad):
    return piece_grad.astype(jnp.bfloat16).reshape(-1)


def body(tokens, cotangent, segment_ids, master, first_moment, second_moment, step_count, rates):
    gathered = gather_weights(master)
    (
        in_projection,
        out_projection,
        filter_taps,
        filter_bias,
        norm_gain,
        gate_gain,
        step_bias,
        log_decay,
        skip_weight,
    ) = unpack(gathered)
    residual = tokens.astype(jnp.float32)
    normed, norm_pullback = jax.vjp(prenorm, residual, norm_gain.astype(jnp.float32))
    normed_low = normed.astype(jnp.bfloat16)
    projected = jnp.dot(normed_low, in_projection, preferred_element_type=jnp.float32)
    mixer_out, mixer_pullback = jax.vjp(
        functools.partial(mixer, segment_ids),
        projected,
        filter_taps.astype(jnp.float32),
        filter_bias.astype(jnp.float32),
        step_bias.astype(jnp.float32),
        log_decay.astype(jnp.float32),
        skip_weight.astype(jnp.float32),
        gate_gain.astype(jnp.float32),
    )
    mixer_low = mixer_out.astype(jnp.bfloat16)
    grad_out = flat_low(contract(mixer_low, cotangent, 0, 0))
    grad_mixer = contract(cotangent, out_projection, 1, 1)
    grad_out, grad_mixer = lax.optimization_barrier((grad_out, grad_mixer))
    out_sum = lax.psum(grad_out, ("rep", "zero"))
    branch = jnp.dot(mixer_low, out_projection, preferred_element_type=jnp.float32)
    mixed = (residual + branch).astype(jnp.bfloat16)
    grad_projected, grad_taps, grad_bias, grad_step_bias, grad_decay, grad_skip, grad_gate_gain = (
        mixer_pullback(grad_mixer)
    )
    projected_low = grad_projected.astype(jnp.bfloat16)
    grad_in = contract(normed_low, projected_low, 0, 0)
    grad_normed = contract(projected_low, in_projection, 1, 1)
    grad_residual, grad_norm_gain = norm_pullback(grad_normed)
    input_grad = (cotangent.astype(jnp.float32) + grad_residual).astype(jnp.bfloat16)
    small = [
        grad_taps,
        grad_bias,
        grad_norm_gain,
        grad_gate_gain,
        grad_step_bias,
        grad_decay,
        grad_skip,
    ]
    late = jnp.concatenate([flat_low(grad_in)] + [flat_low(piece) for piece in small])
    late, out_sum = lax.optimization_barrier((late, out_sum))
    late_sum = lax.psum(late, ("rep", "zero"))
    used_in = grad_in.size
    shard_size = master.shape[0]
    gradient = assemble_gradient(
        [late_sum[:used_in], out_sum, late_sum[used_in:]], shard_size
    ).astype(jnp.float32)
    shard_start = lax.axis_index("zero") * shard_size
    new_first, new_second, new_master = adamw(
        gradient, first_moment, second_moment, master, shard_start, step_count, rates
    )
    return (mixed, input_grad, new_first, new_second, new_master)


def solution(mesh):
    in_specs = (
        P(("rep", "zero"), None),
        P(("rep", "zero"), None),
        P(("rep", "zero")),
        P("zero"),
        P("zero"),
        P("zero"),
        P(),
        P(),
    )
    out_specs = (
        P(("rep", "zero"), None),
        P(("rep", "zero"), None),
        P("zero"),
        P("zero"),
        P("zero"),
    )
    return jax.shard_map(body, mesh=mesh, in_specs=in_specs, out_specs=out_specs, check_vma=False)
```
